512 devices in a mesh: pipe: 4 (over z_hi), ctx: 32 (over y, z_lo, core), dp: 4 (over x).
Axes of the slice: x: 4, y: 8, z: 8 (z_hi: 4, z_lo: 2; z = z_hi * 2 + z_lo), core: 2. Of those that a mesh axis runs over, the one named last changes fastest.
Arguments:
- queries: bfloat16 [4, 4, 4096, 4096], P('pipe', 'dp', 'ctx'), may hold values from -7 to 7
- key_input: bfloat16 [4, 4, 4096, 512], P('pipe', 'dp', 'ctx'), may hold values from -4 to 4
- value_input: bfloat16 [4, 4, 4096, 512], P('pipe', 'dp', 'ctx'), may hold values from -6 to 6
- incoming: bfloat16 [4, 4, 4096, 4096], P('pipe', 'dp', 'ctx'), may hold values from -6 to 6
- segments: int32 [4, 4096], P('dp'), may hold values from 0 to 15, never falling along the last dimension, each value on 1 to 512 neighbouring positions
Outputs:
- query_grad: bfloat16 [4, 4, 4096, 4096], P('pipe', 'dp', 'ctx')
- key_grad: bfloat16 [4, 4, 4096, 512], P('pipe', 'dp', 'ctx')
- value_grad: bfloat16 [4, 4, 4096, 512], P('pipe', 'dp', 'ctx')
- bias_grad: float32 [4, 5120], P('pipe')
The draws below stay inside these ranges and needn't reach their ends.
Inputs may be any that keep to these rules, and one draw needn't show every extreme that they name: `segments`: tokens of one document are contiguous; every document holds 1 to 512 tokens and one holds exactly 512.
All inputs are finite; a program needn't handle non-finite values.
Results may differ from the reference program's by a relative error of at most 0.009.
Values may be sent and summed in bfloat16 or wider, within the bound.
No kernel may reach another device: no remote copies, remote signals or barrier semaphores. Data moves between devices by JAX's collectives and lax.ppermute only.
A program may use at most 64 MiB of HBM per device.

```python
import math
import jax
import jax.numpy as jnp
import numpy as np
from jax import lax

ASKER_STREAMS = 32
SHARED_GROUPS = 4
FEATURE_SIZE = 128
QUERY_PER_KEY = 8
DOC_MOST = 512
LOT_POSITIONS = 4096
DOCS = 16
RELAY_PHASES = 4
SMALL_LOTS = 4


def draw_queries(key, part):
    array_dims = (RELAY_PHASES, SMALL_LOTS, LOT_POSITIONS, ASKER_STREAMS, FEATURE_SIZE)
    noise = jnp.clip(jax.random.normal(jax.random.fold_in(key, 11), array_dims, jnp.float32), -4.0, 4.0)
    value_tensor = noise
    return value_tensor.reshape(RELAY_PHASES, SMALL_LOTS, LOT_POSITIONS, ASKER_STREAMS * FEATURE_SIZE).astype(jnp.bfloat16)


def draw_key_input(key, part):
    array_dims = (RELAY_PHASES, SMALL_LOTS, LOT_POSITIONS, SHARED_GROUPS, FEATURE_SIZE)
    noise = jnp.clip(jax.random.normal(jax.random.fold_in(key, 21), array_dims, jnp.float32), -4.0, 4.0)
    value_tensor = noise
    return value_tensor.reshape(RELAY_PHASES, SMALL_LOTS, LOT_POSITIONS, SHARED_GROUPS * FEATURE_SIZE).astype(jnp.bfloat16)


def level_of(stream_key, shape, shards, least, high):
    gain = 1.0
    for axis_at, shards_of in shards:
        steps = jax.random.uniform(jax.random.fold_in(jax.random.fold_in(stream_key, 6), axis_at), (shards_of,), jnp.float32, least / len(shards), high / len(shards))
        gain = gain * jnp.repeat(jnp.exp(steps), shape[axis_at] // shards_of).reshape((-1,) + (1,) * (len(shape) - 1 - axis_at))
    return gain


def profile(number_of, total, limit, lean):
    weights = [(1 << 20) // math.isqrt(grade ** lean) + 1 for grade in range(2, number_of + 1)]
    spare, counts = total - limit - (number_of - 1), [1] * (number_of - 1)
    while spare > 0:
        candidates = [i for i in range(number_of - 1) if counts[i] < limit]
        pool, remaining = sum([weights[i] for i in candidates]), spare
        for i in candidates:
            addition = min(limit - counts[i], max(1, remaining * weights[i] // pool), spare)
            counts[i] = counts[i] + addition
            spare = spare - addition
    return np.array([limit] + counts)


def uneven_parts(stream_key, amount, total, most, skew):
    if amount == 2:
        one = jax.random.randint(stream_key, (), max(1, total - most), min(most, total - 1) + 1)
        return jnp.stack([one, total - one])
    lengths = jnp.asarray(profile(amount, total, most, skew), jnp.int32)
    twos = (amount - 1) // 2
    source_of, taker = lengths[1:1 + 2 * twos:2], lengths[2:2 + 2 * twos:2]
    room = jnp.minimum(source_of - 1, most - taker)
    shifted = jax.random.randint(jax.random.fold_in(stream_key, 1), (twos,), 0, 1 << 20) % (room + 1)
    lengths = lengths.at[1:1 + 2 * twos:2].set(source_of - shifted).at[2:2 + 2 * twos:2].set(taker + shifted)
    return lengths[jax.random.permutation(jax.random.fold_in(stream_key, 2), amount)]


def scatter_about(own_key, extent, scale, limit, split=(), kind=jnp.bfloat16):
    array = scale * jax.random.normal(own_key, extent, jnp.float32)
    if split:
        array = array * level_of(own_key, extent, split, -0.22, 0.18)
    return jnp.clip(array, -limit, limit).astype(kind)


def setup_inputs(seed: int = 0) -> dict:
    key_of = jax.random.split(jax.random.key(seed), 6)
    queries = draw_queries(jax.random.fold_in(key_of[5], 71), 0)
    key_input = draw_key_input(jax.random.fold_in(key_of[5], 71), 0)
    value_input = scatter_about(key_of[2], (RELAY_PHASES, SMALL_LOTS, LOT_POSITIONS, SHARED_GROUPS * FEATURE_SIZE), 1.0, 6.0, ((0, 4), (1, 4), (2, 32)))
    incoming = scatter_about(key_of[3], (RELAY_PHASES, SMALL_LOTS, LOT_POSITIONS, ASKER_STREAMS * FEATURE_SIZE), 1.0, 6.0, ((0, 4), (1, 4), (2, 32)))
    segments = jax.vmap(lambda own: jnp.searchsorted(jnp.cumsum(uneven_parts(own, DOCS, LOT_POSITIONS, DOC_MOST, 1)), jnp.arange(LOT_POSITIONS), side="right"))(jax.random.split(key_of[4], SMALL_LOTS)).reshape((SMALL_LOTS, LOT_POSITIONS)).astype(jnp.int32)
    return {"queries": queries, "key_input": key_input, "value_input": value_input, "incoming": incoming, "segments": segments}


def attend(queries, key_rows, value_rows, cotangent, query_doc, key_doc, query_pos, key_pos, scaling):
    queries = queries.astype(jnp.float32)
    key_rows = key_rows.astype(jnp.float32)
    value_rows = value_rows.astype(jnp.float32)
    cotangent = cotangent.astype(jnp.float32)
    scores = jnp.einsum('gqd,kd->gqk', queries, key_rows) * scaling
    visible = (query_doc[:, None] == key_doc[None, :]) & (key_pos[None, :] <= query_pos[:, None])
    scores = jnp.where(visible[None], scores, -1e+30)
    row_max = lax.optimization_barrier(jnp.max(scores, axis=-1, keepdims=True))
    weights = jnp.where(visible[None], jnp.exp(scores - row_max), 0.0)
    probs = weights / lax.optimization_barrier(jnp.sum(weights, axis=-1, keepdims=True))
    probs_b = lax.optimization_barrier(probs.astype(jnp.bfloat16)).astype(jnp.float32)
    attn_out = jnp.einsum('gqk,kd->gqd', probs_b, value_rows)
    dot_out = lax.optimization_barrier(jnp.sum(cotangent * attn_out, axis=-1, keepdims=True))
    grad_prob = jnp.einsum('gqd,kd->gqk', cotangent, value_rows)
    grad_score = (probs * (grad_prob - dot_out) * scaling).astype(jnp.bfloat16)
    grad_score = lax.optimization_barrier(grad_score).astype(jnp.float32)
    asker_derivative = jnp.einsum('gqk,kd->gqd', grad_score, key_rows)
    lookup_derivative = jnp.einsum('gqk,gqd->kd', grad_score, queries)
    content_derivative = jnp.einsum('gqk,gqd->kd', probs_b, cotangent)
    return (asker_derivative, lookup_derivative, content_derivative)

def banded(queries, key_rows, value_rows, cotangent, doc_ids, block_len, scaling):
    length = doc_ids.shape[0]
    blocks = length // block_len
    width = key_rows.shape[1]
    key_pad = jnp.concatenate([jnp.zeros((block_len, width), key_rows.dtype), key_rows], axis=0)
    value_pad = jnp.concatenate([jnp.zeros((block_len, width), value_rows.dtype), value_rows], axis=0)
    doc_pad = jnp.concatenate([jnp.full((block_len,), -1, jnp.int32), doc_ids.astype(jnp.int32)])
    pos_pad = jnp.arange(length + block_len, dtype=jnp.int32) - block_len

    def step(carried, block):
        key_acc, value_acc = carried
        anchor = (block * block_len).astype(jnp.int32)
        query_blk = lax.dynamic_slice_in_dim(queries, anchor, block_len, 1)
        cot_blk = lax.dynamic_slice_in_dim(cotangent, anchor, block_len, 1)
        key_blk = lax.dynamic_slice_in_dim(key_pad, anchor, 2 * block_len, 0)
        value_blk = lax.dynamic_slice_in_dim(value_pad, anchor, 2 * block_len, 0)
        query_doc = lax.dynamic_slice_in_dim(doc_ids.astype(jnp.int32), anchor, block_len, 0)
        key_doc = lax.dynamic_slice_in_dim(doc_pad, anchor, 2 * block_len, 0)
        query_pos = anchor + jnp.arange(block_len, dtype=jnp.int32)
        key_pos = lax.dynamic_slice_in_dim(pos_pad, anchor, 2 * block_len, 0)
        asker_derivative, lookup_derivative, content_derivative = attend(query_blk, key_blk, value_blk, cot_blk, query_doc, key_doc, query_pos, key_pos, scaling)
        key_acc = lax.dynamic_update_slice_in_dim(key_acc, lax.dynamic_slice_in_dim(key_acc, anchor, 2 * block_len, 0) + lookup_derivative, anchor, 0)
        value_acc = lax.dynamic_update_slice_in_dim(value_acc, lax.dynamic_slice_in_dim(value_acc, anchor, 2 * block_len, 0) + content_derivative, anchor, 0)
        return ((key_acc, value_acc), asker_derivative)
    start_acc = jnp.zeros((length + block_len, width), jnp.float32)
    (key_acc, value_acc), query_blocks = lax.scan(step, (start_acc, start_acc), jnp.arange(blocks, dtype=jnp.int32))
    groups = queries.shape[0]
    asker_derivative = query_blocks.transpose(1, 0, 2, 3).reshape(groups, length, width)
    return (asker_derivative, key_acc[block_len:], value_acc[block_len:])

def reference(queries, key_input, value_input, incoming, segments):
    scaling = 1.0 / math.sqrt(FEATURE_SIZE)
    grad_q_all, grad_k_all, grad_v_all, offset_entire = ([], [], [], [])
    for phase_index in range(RELAY_PHASES):
        phase_q, phase_k, phase_v = ([], [], [])
        offset_parts = jnp.zeros(((ASKER_STREAMS + 2 * SHARED_GROUPS) * FEATURE_SIZE,), jnp.float32)
        for micro_batch_index in range(SMALL_LOTS):
            query_per_head = queries[phase_index, micro_batch_index].reshape(LOT_POSITIONS, SHARED_GROUPS, QUERY_PER_KEY, FEATURE_SIZE).transpose(1, 2, 0, 3)
            output_grad_heads = incoming[(phase_index + 1) % RELAY_PHASES, micro_batch_index].reshape(LOT_POSITIONS, SHARED_GROUPS, QUERY_PER_KEY, FEATURE_SIZE).transpose(1, 2, 0, 3)
            key_per_head = key_input[phase_index, micro_batch_index].reshape(LOT_POSITIONS, SHARED_GROUPS, FEATURE_SIZE).transpose(1, 0, 2)
            value_per_head = value_input[phase_index, micro_batch_index].reshape(LOT_POSITIONS, SHARED_GROUPS, FEATURE_SIZE).transpose(1, 0, 2)
            doc_ids = segments[micro_batch_index]

            def per_head(members):
                return banded(members[0], members[1], members[2], members[3], doc_ids, DOC_MOST, scaling)
            asker_derivative, lookup_derivative, content_derivative = lax.map(per_head, (query_per_head, key_per_head, value_per_head, output_grad_heads))
            asker_derivative = asker_derivative.transpose(2, 0, 1, 3).reshape(LOT_POSITIONS, ASKER_STREAMS * FEATURE_SIZE)
            lookup_derivative = lookup_derivative.transpose(1, 0, 2).reshape(LOT_POSITIONS, SHARED_GROUPS * FEATURE_SIZE)
            content_derivative = content_derivative.transpose(1, 0, 2).reshape(LOT_POSITIONS, SHARED_GROUPS * FEATURE_SIZE)
            offset_parts = offset_parts + jnp.concatenate([lax.optimization_barrier(jnp.sum(asker_derivative, axis=0)), lax.optimization_barrier(jnp.sum(lookup_derivative, axis=0)), lax.optimization_barrier(jnp.sum(content_derivative, axis=0))])
            phase_q.append(asker_derivative.astype(jnp.bfloat16))
            phase_k.append(lookup_derivative.astype(jnp.bfloat16))
            phase_v.append(content_derivative.astype(jnp.bfloat16))
        grad_q_all.append(jnp.stack(phase_q))
        grad_k_all.append(jnp.stack(phase_k))
        grad_v_all.append(jnp.stack(phase_v))
        offset_entire.append(offset_parts / math.sqrt(SMALL_LOTS * LOT_POSITIONS))
    return (jnp.stack(grad_q_all), jnp.stack(grad_k_all), jnp.stack(grad_v_all), jnp.stack(offset_entire))
```

```python
import math

import jax
import jax.numpy as jnp
from jax import lax
from jax.sharding import PartitionSpec as P

ASKER_STREAMS = 32
SHARED_GROUPS = 4
FEATURE_SIZE = 128
QUERY_PER_KEY = 8


def passed_along(value, axis, steps):
    count = lax.axis_size(axis)
    pairs = [(source, (source + steps) % count) for source in range(count)]
    return lax.ppermute(value, axis, pairs)


def attend(
    queries, key_rows, value_rows, cotangent, query_doc, key_doc, query_pos, key_pos, scaling
):
    scores = (
        jnp.einsum("gqd,kd->gqk", queries, key_rows, preferred_element_type=jnp.float32) * scaling
    )
    visible = (query_doc[:, None] == key_doc[None, :]) & (key_pos[None, :] <= query_pos[:, None])
    scores = jnp.where(visible[None], scores, -1e30)
    row_max = jnp.max(scores, axis=-1, keepdims=True)
    weights = jnp.where(visible[None], jnp.exp(scores - row_max), 0.0)
    probs = weights / jnp.sum(weights, axis=-1, keepdims=True)
    probs_b = probs.astype(jnp.bfloat16)
    attn_out = jnp.einsum("gqk,kd->gqd", probs_b, value_rows, preferred_element_type=jnp.float32)
    dot_out = jnp.sum(cotangent.astype(jnp.float32) * attn_out, axis=-1, keepdims=True)
    grad_prob = jnp.einsum("gqd,kd->gqk", cotangent, value_rows, preferred_element_type=jnp.float32)
    grad_score = (probs * (grad_prob - dot_out) * scaling).astype(jnp.bfloat16)
    asker_derivative = jnp.einsum(
        "gqk,kd->gqd", grad_score, key_rows, preferred_element_type=jnp.float32
    )
    lookup_derivative = jnp.einsum(
        "gqk,gqd->kd", grad_score, queries, preferred_element_type=jnp.float32
    )
    content_derivative = jnp.einsum(
        "gqk,gqd->kd", probs_b, cotangent, preferred_element_type=jnp.float32
    )
    return (asker_derivative, lookup_derivative, content_derivative)


def banded(queries, key_rows, value_rows, cotangent, doc_ids, block_len, scaling):
    length = doc_ids.shape[0]
    blocks = length // block_len
    width = key_rows.shape[1]
    key_pad = jnp.concatenate([jnp.zeros((block_len, width), key_rows.dtype), key_rows], axis=0)
    value_pad = jnp.concatenate(
        [jnp.zeros((block_len, width), value_rows.dtype), value_rows], axis=0
    )
    doc_pad = jnp.concatenate([jnp.full((block_len,), -1, jnp.int32), doc_ids])
    pos_pad = jnp.arange(length + block_len, dtype=jnp.int32) - block_len

    def step(carried, block):
        key_acc, value_acc = carried
        anchor = block * block_len
        query_blk = lax.dynamic_slice_in_dim(queries, anchor, block_len, 1)
        cot_blk = lax.dynamic_slice_in_dim(cotangent, anchor, block_len, 1)
        key_blk = lax.dynamic_slice_in_dim(key_pad, anchor, 2 * block_len, 0)
        value_blk = lax.dynamic_slice_in_dim(value_pad, anchor, 2 * block_len, 0)
        query_doc = lax.dynamic_slice_in_dim(doc_ids, anchor, block_len, 0)
        key_doc = lax.dynamic_slice_in_dim(doc_pad, anchor, 2 * block_len, 0)
        query_pos = anchor + jnp.arange(block_len, dtype=jnp.int32)
        key_pos = lax.dynamic_slice_in_dim(pos_pad, anchor, 2 * block_len, 0)
        asker_derivative, lookup_derivative, content_derivative = attend(
            query_blk, key_blk, value_blk, cot_blk, query_doc, key_doc, query_pos, key_pos, scaling
        )
        key_acc = lax.dynamic_update_slice_in_dim(
            key_acc,
            lax.dynamic_slice_in_dim(key_acc, anchor, 2 * block_len, 0) + lookup_derivative,
            anchor,
            0,
        )
        value_acc = lax.dynamic_update_slice_in_dim(
            value_acc,
            lax.dynamic_slice_in_dim(value_acc, anchor, 2 * block_len, 0) + content_derivative,
            anchor,
            0,
        )
        return ((key_acc, value_acc), asker_derivative)

    start_acc = jnp.zeros((length + block_len, width), jnp.float32)
    (key_acc, value_acc), query_blocks = lax.scan(
        step, (start_acc, start_acc), jnp.arange(blocks, dtype=jnp.int32)
    )
    groups = queries.shape[0]
    asker_derivative = query_blocks.transpose(1, 0, 2, 3).reshape(groups, length, width)
    return (asker_derivative, key_acc[block_len:], value_acc[block_len:])


def body(queries, key_input, value_input, incoming, segments):
    shard_length = queries.shape[2]
    ctx_size = lax.axis_size("ctx")
    reach_dev = min(4, ctx_size - 1)
    block_len = reach_dev * shard_length
    scaling = 1.0 / math.sqrt(FEATURE_SIZE)
    doc_ids = segments[0]
    handed = passed_along(incoming, "pipe", -1)
    query_tok = queries[0, 0].reshape(shard_length, ASKER_STREAMS, FEATURE_SIZE)
    cot_tok = handed[0, 0].reshape(shard_length, ASKER_STREAMS, FEATURE_SIZE)
    key_widened = jnp.repeat(
        key_input[0, 0].reshape(shard_length, SHARED_GROUPS, FEATURE_SIZE), QUERY_PER_KEY, axis=1
    )
    value_widened = jnp.repeat(
        value_input[0, 0].reshape(shard_length, SHARED_GROUPS, FEATURE_SIZE), QUERY_PER_KEY, axis=1
    )
    query_head, key_head, value_head, cot_head = (
        lax.all_to_all(query_tok, "ctx", split_axis=1, concat_axis=0, tiled=True),
        lax.all_to_all(key_widened, "ctx", split_axis=1, concat_axis=0, tiled=True),
        lax.all_to_all(value_widened, "ctx", split_axis=1, concat_axis=0, tiled=True),
        lax.all_to_all(cot_tok, "ctx", split_axis=1, concat_axis=0, tiled=True),
    )

    def per_head(members):
        return banded(
            members[0][None], members[1], members[2], members[3][None], doc_ids, block_len, scaling
        )

    asker_derivative, lookup_derivative, content_derivative = lax.map(
        per_head,
        (
            query_head.transpose(1, 0, 2),
            key_head.transpose(1, 0, 2),
            value_head.transpose(1, 0, 2),
            cot_head.transpose(1, 0, 2),
        ),
    )
    asker_derivative = asker_derivative[:, 0].transpose(1, 0, 2)
    lookup_derivative = lookup_derivative.transpose(1, 0, 2)
    content_derivative = content_derivative.transpose(1, 0, 2)
    query_back, key_backward, value_backward = (
        lax.all_to_all(asker_derivative, "ctx", split_axis=0, concat_axis=1, tiled=True),
        lax.all_to_all(lookup_derivative, "ctx", split_axis=0, concat_axis=1, tiled=True),
        lax.all_to_all(content_derivative, "ctx", split_axis=0, concat_axis=1, tiled=True),
    )
    query_flat = query_back.reshape(shard_length, ASKER_STREAMS * FEATURE_SIZE)
    key_flattened = (
        key_backward.reshape(shard_length, SHARED_GROUPS, QUERY_PER_KEY, FEATURE_SIZE)
        .sum(axis=2)
        .reshape(shard_length, SHARED_GROUPS * FEATURE_SIZE)
    )
    value_flat = (
        value_backward.reshape(shard_length, SHARED_GROUPS, QUERY_PER_KEY, FEATURE_SIZE)
        .sum(axis=2)
        .reshape(shard_length, SHARED_GROUPS * FEATURE_SIZE)
    )
    offset_parts = jnp.concatenate(
        [jnp.sum(query_flat, axis=0), jnp.sum(key_flattened, axis=0), jnp.sum(value_flat, axis=0)]
    )
    pipe_idx = lax.axis_index("pipe")
    slots = jnp.zeros((lax.axis_size("pipe"), offset_parts.shape[0]), jnp.float32).at[pipe_idx].set(offset_parts)
    offset_overall = lax.psum(slots, ("pipe", "ctx", "dp"))[pipe_idx]
    bias_scaled = offset_overall / math.sqrt(lax.axis_size("dp") * shard_length * ctx_size)
    query_grad = query_flat.astype(jnp.bfloat16)[None, None]
    key_grad = key_flattened.astype(jnp.bfloat16)[None, None]
    value_grad = value_flat.astype(jnp.bfloat16)[None, None]
    return (query_grad, key_grad, value_grad, bias_scaled[None])


def solution(mesh):
    return jax.shard_map(
        body,
        mesh=mesh,
        in_specs=(
            P("pipe", "dp", "ctx", None),
            P("pipe", "dp", "ctx", None),
            P("pipe", "dp", "ctx", None),
            P("pipe", "dp", "ctx", None),
            P("dp", None),
        ),
        out_specs=(
            P("pipe", "dp", "ctx", None),
            P("pipe", "dp", "ctx", None),
            P("pipe", "dp", "ctx", None),
            P("pipe", None),
        ),
        check_vma=False,
    )
```

```python
import math

import jax
import jax.numpy as jnp
from jax import lax
from jax.sharding import PartitionSpec as P

ASKER_STREAMS = 32
SHARED_GROUPS = 4
FEATURE_SIZE = 128
QUERY_PER_KEY = 8
DOC_MOST = 512


def passed_along(value, axis, steps):
    count = lax.axis_size(axis)
    pairs = [(source, (source + steps) % count) for source in range(count)]
    return lax.ppermute(value, axis, pairs)


def shifted(value, axis, steps):
    count = lax.axis_size(axis)
    pairs = [(source, source + steps) for source in range(count) if 0 <= source + steps < count]
    return lax.ppermute(value, axis, pairs)


def butterfly_sum(value, axis):
    count = lax.axis_size(axis)
    if count & (count - 1):
        return lax.psum(value, axis)
    stride = 1
    while stride < count:
        pairs = [(source, source ^ stride) for source in range(count)]
        value = value + lax.ppermute(value, axis, pairs)
        stride *= 2
    return value


def attend_group(query_g, key_g, value_g, cot_g, visible, scaling):
    scores = (
        jnp.einsum("qhd,kd->hqk", query_g, key_g, preferred_element_type=jnp.float32) * scaling
    )
    scores = jnp.where(visible[None], scores, -1e30)
    row_max = jnp.max(scores, axis=-1, keepdims=True)
    weights = jnp.where(visible[None], jnp.exp(scores - row_max), 0.0)
    probs = weights / jnp.sum(weights, axis=-1, keepdims=True)
    probs_b = probs.astype(jnp.bfloat16)
    attn_out = jnp.einsum("hqk,kd->qhd", probs_b, value_g, preferred_element_type=jnp.float32)
    dot_out = jnp.sum(cot_g.astype(jnp.float32) * attn_out, axis=-1).T[:, :, None]
    grad_prob = jnp.einsum("qhd,kd->hqk", cot_g, value_g, preferred_element_type=jnp.float32)
    grad_score = (probs * (grad_prob - dot_out) * scaling).astype(jnp.bfloat16)
    asker = jnp.einsum("hqk,kd->qhd", grad_score, key_g, preferred_element_type=jnp.float32)
    lookup = jnp.einsum("hqk,qhd->kd", grad_score, query_g, preferred_element_type=jnp.float32)
    content = jnp.einsum("hqk,qhd->kd", probs_b, cot_g, preferred_element_type=jnp.float32)
    return asker, lookup, content


def body(queries, key_input, value_input, incoming, segments):
    shard_length = queries.shape[2]
    ctx_size = lax.axis_size("ctx")
    reach = min(-(-(DOC_MOST - 1) // shard_length), ctx_size - 1)
    window = (reach + 1) * shard_length
    width = SHARED_GROUPS * FEATURE_SIZE
    scaling = 1.0 / math.sqrt(FEATURE_SIZE)
    here = lax.axis_index("ctx")
    anchor = here * shard_length

    handed = passed_along(incoming, "pipe", -1)
    kv_own = jnp.concatenate([key_input[0, 0], value_input[0, 0]], axis=1)
    kv_window = jnp.concatenate(
        [shifted(kv_own, "ctx", steps) for steps in range(reach, 0, -1)] + [kv_own], axis=0
    )

    doc_ids = segments[0]
    doc_pad = jnp.concatenate([jnp.full((reach * shard_length,), -1, jnp.int32), doc_ids])
    key_doc = lax.dynamic_slice_in_dim(doc_pad, anchor, window, 0)
    query_doc = lax.dynamic_slice_in_dim(doc_ids, anchor, shard_length, 0)
    query_pos = jnp.arange(shard_length, dtype=jnp.int32) + reach * shard_length
    key_pos = jnp.arange(window, dtype=jnp.int32)
    visible = (query_doc[:, None] == key_doc[None, :]) & (key_pos[None, :] <= query_pos[:, None])

    query_tok = queries[0, 0].reshape(shard_length, ASKER_STREAMS, FEATURE_SIZE)
    cot_tok = handed[0, 0].reshape(shard_length, ASKER_STREAMS, FEATURE_SIZE)
    askers, lookups, contents = [], [], []
    for group in range(SHARED_GROUPS):
        heads = slice(group * QUERY_PER_KEY, (group + 1) * QUERY_PER_KEY)
        cols = slice(group * FEATURE_SIZE, (group + 1) * FEATURE_SIZE)
        vcols = slice(width + group * FEATURE_SIZE, width + (group + 1) * FEATURE_SIZE)
        asker, lookup, content = attend_group(
            query_tok[:, heads],
            kv_window[:, cols],
            kv_window[:, vcols],
            cot_tok[:, heads],
            visible,
            scaling,
        )
        askers.append(asker)
        lookups.append(lookup)
        contents.append(content)
    query_flat = jnp.concatenate(askers, axis=1).reshape(shard_length, ASKER_STREAMS * FEATURE_SIZE)
    grad_window = jnp.concatenate(lookups + contents, axis=1)

    offset_parts = jnp.concatenate([jnp.sum(query_flat, axis=0), jnp.sum(grad_window, axis=0)])
    offset_overall = butterfly_sum(butterfly_sum(offset_parts, "ctx"), "dp")
    bias_scaled = offset_overall / math.sqrt(lax.axis_size("dp") * shard_length * ctx_size)

    grad_own = grad_window[reach * shard_length :]
    for block in range(reach):
        steps = reach - block
        grad_own = grad_own + shifted(
            grad_window[block * shard_length : (block + 1) * shard_length], "ctx", -steps
        )

    query_grad = query_flat.astype(jnp.bfloat16)[None, None]
    key_grad = grad_own[:, :width].astype(jnp.bfloat16)[None, None]
    value_grad = grad_own[:, width:].astype(jnp.bfloat16)[None, None]
    return (query_grad, key_grad, value_grad, bias_scaled[None])


def solution(mesh):
    return jax.shard_map(
        body,
        mesh=mesh,
        in_specs=(
            P("pipe", "dp", "ctx", None),
            P("pipe", "dp", "ctx", None),
            P("pipe", "dp", "ctx", None),
            P("pipe", "dp", "ctx", None),
            P("dp", None),
        ),
        out_specs=(
            P("pipe", "dp", "ctx", None),
            P("pipe", "dp", "ctx", None),
            P("pipe", "dp", "ctx", None),
            P("pipe", None),
        ),
        check_vma=False,
    )
```

```python
import math

import jax
import jax.numpy as jnp
from jax import lax
from jax.sharding import PartitionSpec as P

ASKER_STREAMS = 32
SHARED_GROUPS = 4
FEATURE_SIZE = 128
QUERY_PER_KEY = 8
DOC_MOST = 512


def passed_along(value, axis, steps):
    count = lax.axis_size(axis)
    pairs = [(source, (source + steps) % count) for source in range(count)]
    return lax.ppermute(value, axis, pairs)


def shifted(value, axis, steps):
    count = lax.axis_size(axis)
    pairs = [(source, source + steps) for source in range(count) if 0 <= source + steps < count]
    return lax.ppermute(value, axis, pairs)


def radix_rounds(count):
    rounds, stride = [], 1
    while stride < count:
        radix = 4 if count % (stride * 4) == 0 else 2
        rounds.append((stride, radix))
        stride *= radix
    return rounds


def group_sum(value, axis):
    count = lax.axis_size(axis)
    if count & (count - 1):
        return lax.psum(value, axis)
    here = lax.axis_index(axis)
    for stride, radix in radix_rounds(count):
        got = [value] + [
            lax.ppermute(value, axis, [(i, i ^ (t * stride)) for i in range(count)])
            for t in range(1, radix)
        ]
        stack = jnp.stack(got)
        spot = (here // stride) % radix
        ordered = jnp.take(stack, spot ^ jnp.arange(radix), axis=0)
        while ordered.shape[0] > 1:
            ordered = ordered[0::2] + ordered[1::2]
        value = ordered[0]
    return value


def attend_group(query_g, key_g, value_g, cot_g, visible, scaling):
    scores = (
        jnp.einsum("qhd,kd->hqk", query_g, key_g, preferred_element_type=jnp.float32) * scaling
    )
    scores = jnp.where(visible[None], scores, -1e30)
    row_max = jnp.max(scores, axis=-1, keepdims=True)
    weights = jnp.where(visible[None], jnp.exp(scores - row_max), 0.0)
    probs = weights / jnp.sum(weights, axis=-1, keepdims=True)
    probs_b = probs.astype(jnp.bfloat16)
    attn_out = jnp.einsum("hqk,kd->qhd", probs_b, value_g, preferred_element_type=jnp.float32)
    dot_out = jnp.sum(cot_g.astype(jnp.float32) * attn_out, axis=-1).T[:, :, None]
    grad_prob = jnp.einsum("qhd,kd->hqk", cot_g, value_g, preferred_element_type=jnp.float32)
    grad_score = (probs * (grad_prob - dot_out) * scaling).astype(jnp.bfloat16)
    asker = jnp.einsum("hqk,kd->qhd", grad_score, key_g, preferred_element_type=jnp.float32)
    lookup = jnp.einsum("hqk,qhd->kd", grad_score, query_g, preferred_element_type=jnp.float32)
    content = jnp.einsum("hqk,qhd->kd", probs_b, cot_g, preferred_element_type=jnp.float32)
    return asker, lookup, content


def body(queries, key_input, value_input, incoming, segments):
    shard_length = queries.shape[2]
    ctx_size = lax.axis_size("ctx")
    reach = min(-(-(DOC_MOST - 1) // shard_length), ctx_size - 1)
    window = (reach + 1) * shard_length
    width = SHARED_GROUPS * FEATURE_SIZE
    scaling = 1.0 / math.sqrt(FEATURE_SIZE)
    here = lax.axis_index("ctx")
    anchor = here * shard_length

    group_cols = QUERY_PER_KEY * FEATURE_SIZE
    cot_groups = [
        passed_along(incoming[0, 0, :, g * group_cols : (g + 1) * group_cols], "pipe", -1)
        for g in range(SHARED_GROUPS)
    ]
    kv_own = jnp.concatenate([key_input[0, 0], value_input[0, 0]], axis=1)
    kv_window = jnp.concatenate(
        [shifted(kv_own, "ctx", steps) for steps in range(reach, 0, -1)] + [kv_own], axis=0
    )

    doc_ids = segments[0]
    doc_pad = jnp.concatenate([jnp.full((reach * shard_length,), -1, jnp.int32), doc_ids])
    key_doc = lax.dynamic_slice_in_dim(doc_pad, anchor, window, 0)
    query_doc = lax.dynamic_slice_in_dim(doc_ids, anchor, shard_length, 0)
    query_pos = jnp.arange(shard_length, dtype=jnp.int32) + reach * shard_length
    key_pos = jnp.arange(window, dtype=jnp.int32)
    visible = (query_doc[:, None] == key_doc[None, :]) & (key_pos[None, :] <= query_pos[:, None])

    query_tok = queries[0, 0].reshape(shard_length, ASKER_STREAMS, FEATURE_SIZE)
    askers, lookups, contents = [], [], []
    for group in range(SHARED_GROUPS):
        heads = slice(group * QUERY_PER_KEY, (group + 1) * QUERY_PER_KEY)
        cols = slice(group * FEATURE_SIZE, (group + 1) * FEATURE_SIZE)
        vcols = slice(width + group * FEATURE_SIZE, width + (group + 1) * FEATURE_SIZE)
        asker, lookup, content = attend_group(
            query_tok[:, heads],
            kv_window[:, cols],
            kv_window[:, vcols],
            cot_groups[group].reshape(shard_length, QUERY_PER_KEY, FEATURE_SIZE),
            visible,
            scaling,
        )
        askers.append(asker)
        lookups.append(lookup)
        contents.append(content)
    query_flat = jnp.concatenate(askers, axis=1).reshape(shard_length, ASKER_STREAMS * FEATURE_SIZE)
    grad_window = jnp.concatenate(lookups + contents, axis=1)

    offset_parts = jnp.concatenate([jnp.sum(query_flat, axis=0), jnp.sum(grad_window, axis=0)])
    offset_overall = group_sum(group_sum(offset_parts, "ctx"), "dp")
    bias_scaled = offset_overall / math.sqrt(lax.axis_size("dp") * shard_length * ctx_size)

    grad_own = grad_window[reach * shard_length :]
    for block in range(reach):
        steps = reach - block
        grad_own = grad_own + shifted(
            grad_window[block * shard_length : (block + 1) * shard_length], "ctx", -steps
        )

    query_grad = query_flat.astype(jnp.bfloat16)[None, None]
    key_grad = grad_own[:, :width].astype(jnp.bfloat16)[None, None]
    value_grad = grad_own[:, width:].astype(jnp.bfloat16)[None, None]
    return (query_grad, key_grad, value_grad, bias_scaled[None])


def solution(mesh):
    return jax.shard_map(
        body,
        mesh=mesh,
        in_specs=(
            P("pipe", "dp", "ctx", None),
            P("pipe", "dp", "ctx", None),
            P("pipe", "dp", "ctx", None),
            P("pipe", "dp", "ctx", None),
            P("dp", None),
        ),
        out_specs=(
            P("pipe", "dp", "ctx", None),
            P("pipe", "dp", "ctx", None),
            P("pipe", "dp", "ctx", None),
            P("pipe", None),
        ),
        check_vma=False,
    )
```

```python
import math

import jax
import jax.numpy as jnp
from jax import lax
from jax.sharding import PartitionSpec as P


ASKER_STREAMS = 32
SHARED_GROUPS = 4
FEATURE_SIZE = 128
QUERY_PER_KEY = 8
DOC_MOST = 512


def passed_along(value, axis, steps):
    count = lax.axis_size(axis)
    pairs = [(source, (source + steps) % count) for source in range(count)]
    return lax.ppermute(value, axis, pairs)


def shifted(value, axis, steps):
    count = lax.axis_size(axis)
    pairs = [(source, source + steps) for source in range(count) if 0 <= source + steps < count]
    return lax.ppermute(value, axis, pairs)


def radix_rounds(count):
    rounds, stride = [], 1
    while stride < count:
        radix = 4 if count % (stride * 4) == 0 else 2
        rounds.append((stride, radix))
        stride *= radix
    return rounds


def group_sum(value, axis):
    count = lax.axis_size(axis)
    if count & (count - 1):
        return lax.psum(value, axis)
    here = lax.axis_index(axis)
    for stride, radix in radix_rounds(count):
        got = [value] + [
            lax.ppermute(value, axis, [(i, i ^ (t * stride)) for i in range(count)])
            for t in range(1, radix)
        ]
        stack = jnp.stack(got)
        spot = (here // stride) % radix
        ordered = jnp.take(stack, spot ^ jnp.arange(radix), axis=0)
        while ordered.shape[0] > 1:
            ordered = ordered[0::2] + ordered[1::2]
        value = ordered[0]
    return value


def attend_group(query_g, key_g, value_g, cot_g, visible, scaling):
    scores = (
        jnp.einsum("qhd,kd->hqk", query_g, key_g, preferred_element_type=jnp.float32) * scaling
    )
    scores = jnp.where(visible[None], scores, -1e30)
    row_max = jnp.max(scores, axis=-1, keepdims=True)
    weights = jnp.where(visible[None], jnp.exp(scores - row_max), 0.0)
    probs = weights / jnp.sum(weights, axis=-1, keepdims=True)
    probs_b = probs.astype(jnp.bfloat16)
    attn_out = jnp.einsum("hqk,kd->qhd", probs_b, value_g, preferred_element_type=jnp.float32)
    dot_out = jnp.sum(cot_g.astype(jnp.float32) * attn_out, axis=-1).T[:, :, None]
    grad_prob = jnp.einsum("qhd,kd->hqk", cot_g, value_g, preferred_element_type=jnp.float32)
    grad_score = (probs * (grad_prob - dot_out) * scaling).astype(jnp.bfloat16)
    asker = jnp.einsum("hqk,kd->qhd", grad_score, key_g, preferred_element_type=jnp.float32)
    lookup = jnp.einsum("hqk,qhd->kd", grad_score, query_g, preferred_element_type=jnp.float32)
    content = jnp.einsum("hqk,qhd->kd", probs_b, cot_g, preferred_element_type=jnp.float32)
    return asker, lookup, content


def body_inner(queries, key_input, value_input, incoming, segments):
    shard_length = queries.shape[2]
    ctx_size = lax.axis_size("ctx")
    reach = min(-(-(DOC_MOST - 1) // shard_length), ctx_size - 1)
    window = (reach + 1) * shard_length
    width = SHARED_GROUPS * FEATURE_SIZE
    scaling = 1.0 / math.sqrt(FEATURE_SIZE)
    here = lax.axis_index("ctx")
    anchor = here * shard_length

    group_cols = QUERY_PER_KEY * FEATURE_SIZE
    cot_groups = [
        passed_along(incoming[0, 0, :, g * group_cols : (g + 1) * group_cols], "pipe", -1)
        for g in range(SHARED_GROUPS)
    ]
    kv_own = jnp.concatenate([key_input[0, 0], value_input[0, 0]], axis=1)
    kv_window = jnp.concatenate(
        [shifted(kv_own, "ctx", steps) for steps in range(reach, 0, -1)] + [kv_own], axis=0
    )

    doc_ids = segments[0]
    doc_pad = jnp.concatenate([jnp.full((reach * shard_length,), -1, jnp.int32), doc_ids])
    key_doc = lax.dynamic_slice_in_dim(doc_pad, anchor, window, 0)
    query_doc = lax.dynamic_slice_in_dim(doc_ids, anchor, shard_length, 0)
    query_pos = jnp.arange(shard_length, dtype=jnp.int32) + reach * shard_length
    key_pos = jnp.arange(window, dtype=jnp.int32)
    visible = (query_doc[:, None] == key_doc[None, :]) & (key_pos[None, :] <= query_pos[:, None])

    query_tok = queries[0, 0].reshape(shard_length, ASKER_STREAMS, FEATURE_SIZE)
    askers, lookups, contents = [], [], []
    for group in range(SHARED_GROUPS):
        heads = slice(group * QUERY_PER_KEY, (group + 1) * QUERY_PER_KEY)
        cols = slice(group * FEATURE_SIZE, (group + 1) * FEATURE_SIZE)
        vcols = slice(width + group * FEATURE_SIZE, width + (group + 1) * FEATURE_SIZE)
        asker, lookup, content = attend_group(
            query_tok[:, heads],
            kv_window[:, cols],
            kv_window[:, vcols],
            cot_groups[group].reshape(shard_length, QUERY_PER_KEY, FEATURE_SIZE),
            visible,
            scaling,
        )
        askers.append(asker)
        lookups.append(lookup)
        contents.append(content)
    query_flat = jnp.concatenate(askers, axis=1).reshape(shard_length, ASKER_STREAMS * FEATURE_SIZE)
    grad_window = jnp.concatenate(lookups + contents, axis=1)

    offset_parts = jnp.concatenate([jnp.sum(query_flat, axis=0), jnp.sum(grad_window, axis=0)])

    grad_own = grad_window[reach * shard_length :]
    for block in range(reach):
        steps = reach - block
        part = grad_window[block * shard_length : (block + 1) * shard_length]
        grad_own = grad_own + shifted(part.astype(jnp.bfloat16), "ctx", -steps).astype(jnp.float32)

    offset_overall = group_sum(group_sum(offset_parts, "ctx"), "dp")
    bias_scaled = offset_overall / math.sqrt(lax.axis_size("dp") * shard_length * ctx_size)

    query_grad = query_flat.astype(jnp.bfloat16)[None, None]
    key_grad = grad_own[:, :width].astype(jnp.bfloat16)[None, None]
    value_grad = grad_own[:, width:].astype(jnp.bfloat16)[None, None]
    return (query_grad, key_grad, value_grad, bias_scaled[None])


def solution(mesh):
    return jax.shard_map(
        body_inner,
        mesh=mesh,
        in_specs=(
            P("pipe", "dp", "ctx", None),
            P("pipe", "dp", "ctx", None),
            P("pipe", "dp", "ctx", None),
            P("pipe", "dp", "ctx", None),
            P("dp", None),
        ),
        out_specs=(
            P("pipe", "dp", "ctx", None),
            P("pipe", "dp", "ctx", None),
            P("pipe", "dp", "ctx", None),
            P("pipe", None),
        ),
        check_vma=False,
    )
```

```python
import math

import jax
import jax.numpy as jnp
from jax import lax
from jax.sharding import PartitionSpec as P


ASKER_STREAMS = 32
SHARED_GROUPS = 4
FEATURE_SIZE = 128
QUERY_PER_KEY = 8
DOC_MOST = 512


def passed_along(value, axis, steps):
    count = lax.axis_size(axis)
    pairs = [(source, (source + steps) % count) for source in range(count)]
    return lax.ppermute(value, axis, pairs)


def shifted(value, axis, steps):
    count = lax.axis_size(axis)
    pairs = [(source, source + steps) for source in range(count) if 0 <= source + steps < count]
    return lax.ppermute(value, axis, pairs)


def radix_rounds(count):
    rounds, stride = [], 1
    while stride < count:
        radix = 4 if count % (stride * 4) == 0 else 2
        rounds.append((stride, radix))
        stride *= radix
    return rounds


def group_sum(value, axis):
    count = lax.axis_size(axis)
    if count & (count - 1):
        return lax.psum(value, axis)
    here = lax.axis_index(axis)
    for stride, radix in radix_rounds(count):
        got = [value] + [
            lax.ppermute(value, axis, [(i, i ^ (t * stride)) for i in range(count)])
            for t in range(1, radix)
        ]
        stack = jnp.stack(got)
        spot = (here // stride) % radix
        ordered = jnp.take(stack, spot ^ jnp.arange(radix), axis=0)
        while ordered.shape[0] > 1:
            ordered = ordered[0::2] + ordered[1::2]
        value = ordered[0]
    return value


def exchange_sum(value, axes):
    count = 1
    for axis in axes:
        count *= lax.axis_size(axis)
    if value.shape[0] % count:
        return group_sum(group_sum(value, axes[0]), axes[1])
    pieces = lax.all_to_all(value.reshape(count, -1), axes, 0, 0, tiled=True)
    ordered = pieces
    while ordered.shape[0] > 1:
        if ordered.shape[0] % 2:
            ordered = jnp.concatenate([ordered[:1] + ordered[1:2], ordered[2:]])
        else:
            ordered = ordered[0::2] + ordered[1::2]
    mine = jnp.broadcast_to(ordered, (count, ordered.shape[1]))
    return lax.all_to_all(mine, axes, 0, 0, tiled=True).reshape(-1)


def attend_group(query_g, key_g, value_g, cot_g, visible, scaling):
    scores = (
        jnp.einsum("qhd,kd->hqk", query_g, key_g, preferred_element_type=jnp.float32) * scaling
    )
    scores = jnp.where(visible[None], scores, -1e30)
    row_max = jnp.max(scores, axis=-1, keepdims=True)
    weights = jnp.where(visible[None], jnp.exp(scores - row_max), 0.0)
    probs = weights / jnp.sum(weights, axis=-1, keepdims=True)
    probs_b = probs.astype(jnp.bfloat16)
    attn_out = jnp.einsum("hqk,kd->qhd", probs_b, value_g, preferred_element_type=jnp.float32)
    dot_out = jnp.sum(cot_g.astype(jnp.float32) * attn_out, axis=-1).T[:, :, None]
    grad_prob = jnp.einsum("qhd,kd->hqk", cot_g, value_g, preferred_element_type=jnp.float32)
    grad_score = (probs * (grad_prob - dot_out) * scaling).astype(jnp.bfloat16)
    asker = jnp.einsum("hqk,kd->qhd", grad_score, key_g, preferred_element_type=jnp.float32)
    lookup = jnp.einsum("hqk,qhd->kd", grad_score, query_g, preferred_element_type=jnp.float32)
    content = jnp.einsum("hqk,qhd->kd", probs_b, cot_g, preferred_element_type=jnp.float32)
    return asker, lookup, content


def body_inner(queries, key_input, value_input, incoming, segments):
    shard_length = queries.shape[2]
    ctx_size = lax.axis_size("ctx")
    reach = min(-(-(DOC_MOST - 1) // shard_length), ctx_size - 1)
    window = (reach + 1) * shard_length
    width = SHARED_GROUPS * FEATURE_SIZE
    scaling = 1.0 / math.sqrt(FEATURE_SIZE)
    here = lax.axis_index("ctx")
    anchor = here * shard_length

    group_cols = QUERY_PER_KEY * FEATURE_SIZE
    cot_groups = [
        passed_along(incoming[0, 0, :, g * group_cols : (g + 1) * group_cols], "pipe", -1)
        for g in range(SHARED_GROUPS)
    ]
    kv_own = jnp.concatenate([key_input[0, 0], value_input[0, 0]], axis=1)
    kv_window = jnp.concatenate(
        [shifted(kv_own, "ctx", steps) for steps in range(reach, 0, -1)] + [kv_own], axis=0
    )

    doc_ids = segments[0]
    doc_pad = jnp.concatenate([jnp.full((reach * shard_length,), -1, jnp.int32), doc_ids])
    key_doc = lax.dynamic_slice_in_dim(doc_pad, anchor, window, 0)
    query_doc = lax.dynamic_slice_in_dim(doc_ids, anchor, shard_length, 0)
    query_pos = jnp.arange(shard_length, dtype=jnp.int32) + reach * shard_length
    key_pos = jnp.arange(window, dtype=jnp.int32)
    visible = (query_doc[:, None] == key_doc[None, :]) & (key_pos[None, :] <= query_pos[:, None])

    query_tok = queries[0, 0].reshape(shard_length, ASKER_STREAMS, FEATURE_SIZE)
    askers, lookups, contents = [], [], []
    for group in range(SHARED_GROUPS):
        heads = slice(group * QUERY_PER_KEY, (group + 1) * QUERY_PER_KEY)
        cols = slice(group * FEATURE_SIZE, (group + 1) * FEATURE_SIZE)
        vcols = slice(width + group * FEATURE_SIZE, width + (group + 1) * FEATURE_SIZE)
        asker, lookup, content = attend_group(
            query_tok[:, heads],
            kv_window[:, cols],
            kv_window[:, vcols],
            cot_groups[group].reshape(shard_length, QUERY_PER_KEY, FEATURE_SIZE),
            visible,
            scaling,
        )
        askers.append(asker)
        lookups.append(lookup)
        contents.append(content)
    query_flat = jnp.concatenate(askers, axis=1).reshape(shard_length, ASKER_STREAMS * FEATURE_SIZE)
    grad_window = jnp.concatenate(lookups + contents, axis=1)

    offset_parts = jnp.concatenate([jnp.sum(query_flat, axis=0), jnp.sum(grad_window, axis=0)])

    grad_own = grad_window[reach * shard_length :]
    for block in range(reach):
        steps = reach - block
        part = grad_window[block * shard_length : (block + 1) * shard_length]
        grad_own = grad_own + shifted(part.astype(jnp.bfloat16), "ctx", -steps).astype(jnp.float32)

    offset_overall = exchange_sum(offset_parts, ("ctx", "dp"))
    bias_scaled = offset_overall / math.sqrt(lax.axis_size("dp") * shard_length * ctx_size)

    query_grad = query_flat.astype(jnp.bfloat16)[None, None]
    key_grad = grad_own[:, :width].astype(jnp.bfloat16)[None, None]
    value_grad = grad_own[:, width:].astype(jnp.bfloat16)[None, None]
    return (query_grad, key_grad, value_grad, bias_scaled[None])


def solution(mesh):
    return jax.shard_map(
        body_inner,
        mesh=mesh,
        in_specs=(
            P("pipe", "dp", "ctx", None),
            P("pipe", "dp", "ctx", None),
            P("pipe", "dp", "ctx", None),
            P("pipe", "dp", "ctx", None),
            P("dp", None),
        ),
        out_specs=(
            P("pipe", "dp", "ctx", None),
            P("pipe", "dp", "ctx", None),
            P("pipe", "dp", "ctx", None),
            P("pipe", None),
        ),
        check_vma=False,
    )
```

```python
import math

import jax
import jax.numpy as jnp
from jax import lax
from jax.sharding import PartitionSpec as P


ASKER_STREAMS = 32
SHARED_GROUPS = 4
FEATURE_SIZE = 128
QUERY_PER_KEY = 8
DOC_MOST = 512


def passed_along(value, axis, steps):
    count = lax.axis_size(axis)
    pairs = [(source, (source + steps) % count) for source in range(count)]
    return lax.ppermute(value, axis, pairs)


def shifted(value, axis, steps):
    count = lax.axis_size(axis)
    pairs = [(source, source + steps) for source in range(count) if 0 <= source + steps < count]
    return lax.ppermute(value, axis, pairs)


def radix_rounds(count):
    rounds, stride = [], 1
    while stride < count:
        radix = 4 if count % (stride * 4) == 0 else 2
        rounds.append((stride, radix))
        stride *= radix
    return rounds


def group_sum(value, axis):
    count = lax.axis_size(axis)
    if count & (count - 1):
        return lax.psum(value, axis)
    here = lax.axis_index(axis)
    for stride, radix in radix_rounds(count):
        got = [value] + [
            lax.ppermute(value, axis, [(i, i ^ (t * stride)) for i in range(count)])
            for t in range(1, radix)
        ]
        stack = jnp.stack(got)
        spot = (here // stride) % radix
        ordered = jnp.take(stack, spot ^ jnp.arange(radix), axis=0)
        while ordered.shape[0] > 1:
            ordered = ordered[0::2] + ordered[1::2]
        value = ordered[0]
    return value


def exchange_sum(value, axes):
    count = 1
    for axis in axes:
        count *= lax.axis_size(axis)
    if value.shape[0] % count:
        return group_sum(group_sum(value, axes[0]), axes[1])
    pieces = lax.all_to_all(value.reshape(count, -1), axes, 0, 0, tiled=True)
    ordered = pieces
    while ordered.shape[0] > 1:
        if ordered.shape[0] % 2:
            ordered = jnp.concatenate([ordered[:1] + ordered[1:2], ordered[2:]])
        else:
            ordered = ordered[0::2] + ordered[1::2]
    mine = jnp.broadcast_to(ordered, (count, ordered.shape[1]))
    return lax.all_to_all(mine, axes, 0, 0, tiled=True).reshape(-1)


def attend_group(query_g, key_g, value_g, cot_g, visible, scaling):
    scores = (
        jnp.einsum("qhd,kd->hqk", query_g, key_g, preferred_element_type=jnp.float32) * scaling
    )
    scores = jnp.where(visible[None], scores, -1e30)
    row_max = jnp.max(scores, axis=-1, keepdims=True)
    weights = jnp.where(visible[None], jnp.exp(scores - row_max), 0.0)
    probs = weights / jnp.sum(weights, axis=-1, keepdims=True)
    probs_b = probs.astype(jnp.bfloat16)
    attn_out = jnp.einsum("hqk,kd->qhd", probs_b, value_g, preferred_element_type=jnp.float32)
    dot_out = jnp.sum(cot_g.astype(jnp.float32) * attn_out, axis=-1).T[:, :, None]
    grad_prob = jnp.einsum("qhd,kd->hqk", cot_g, value_g, preferred_element_type=jnp.float32)
    grad_score = (probs * (grad_prob - dot_out) * scaling).astype(jnp.bfloat16)
    asker = jnp.einsum("hqk,kd->qhd", grad_score, key_g, preferred_element_type=jnp.float32)
    lookup = jnp.einsum("hqk,qhd->kd", grad_score, query_g, preferred_element_type=jnp.float32)
    content = jnp.einsum("hqk,qhd->kd", probs_b, cot_g, preferred_element_type=jnp.float32)
    return asker, lookup, content


def body_inner(queries, key_input, value_input, incoming, segments):
    shard_length = queries.shape[2]
    ctx_size = lax.axis_size("ctx")
    reach = min(-(-(DOC_MOST - 1) // shard_length), ctx_size - 1)
    window = (reach + 1) * shard_length
    width = SHARED_GROUPS * FEATURE_SIZE
    scaling = 1.0 / math.sqrt(FEATURE_SIZE)
    here = lax.axis_index("ctx")
    anchor = here * shard_length

    group_cols = QUERY_PER_KEY * FEATURE_SIZE
    cot_groups = []
    for g in range(SHARED_GROUPS):
        cot_groups.append(
            passed_along(incoming[0, 0, :, g * group_cols : (g + 1) * group_cols], "pipe", -1)
        )
    kv_own = jnp.concatenate([key_input[0, 0], value_input[0, 0]], axis=1)
    kv_window = jnp.concatenate(
        [shifted(kv_own, "ctx", steps) for steps in range(reach, 0, -1)] + [kv_own], axis=0
    )

    doc_ids = segments[0]
    doc_pad = jnp.concatenate([jnp.full((reach * shard_length,), -1, jnp.int32), doc_ids])
    key_doc = lax.dynamic_slice_in_dim(doc_pad, anchor, window, 0)
    query_doc = lax.dynamic_slice_in_dim(doc_ids, anchor, shard_length, 0)
    query_pos = jnp.arange(shard_length, dtype=jnp.int32) + reach * shard_length
    key_pos = jnp.arange(window, dtype=jnp.int32)
    visible = (query_doc[:, None] == key_doc[None, :]) & (key_pos[None, :] <= query_pos[:, None])

    query_tok = queries[0, 0].reshape(shard_length, ASKER_STREAMS, FEATURE_SIZE)
    askers, lookups, contents = [], [], []
    for group in range(SHARED_GROUPS):
        heads = slice(group * QUERY_PER_KEY, (group + 1) * QUERY_PER_KEY)
        cols = slice(group * FEATURE_SIZE, (group + 1) * FEATURE_SIZE)
        vcols = slice(width + group * FEATURE_SIZE, width + (group + 1) * FEATURE_SIZE)
        asker, lookup, content = attend_group(
            query_tok[:, heads],
            kv_window[:, cols],
            kv_window[:, vcols],
            cot_groups[group].reshape(shard_length, QUERY_PER_KEY, FEATURE_SIZE),
            visible,
            scaling,
        )
        askers.append(asker)
        lookups.append(lookup)
        contents.append(content)
    query_flat = jnp.concatenate(askers, axis=1).reshape(shard_length, ASKER_STREAMS * FEATURE_SIZE)
    grad_window = jnp.concatenate(lookups + contents, axis=1)

    offset_parts = jnp.concatenate([jnp.sum(query_flat, axis=0), jnp.sum(grad_window, axis=0)])

    grad_own = grad_window[reach * shard_length :]
    for block in range(reach):
        steps = reach - block
        part = grad_window[block * shard_length : (block + 1) * shard_length]
        grad_own = grad_own + shifted(part.astype(jnp.bfloat16), "ctx", -steps).astype(jnp.float32)

    offset_overall = exchange_sum(offset_parts, ("ctx", "dp"))
    bias_scaled = offset_overall / math.sqrt(lax.axis_size("dp") * shard_length * ctx_size)

    query_grad = query_flat.astype(jnp.bfloat16)[None, None]
    key_grad = grad_own[:, :width].astype(jnp.bfloat16)[None, None]
    value_grad = grad_own[:, width:].astype(jnp.bfloat16)[None, None]
    return (query_grad, key_grad, value_grad, bias_scaled[None])


def solution(mesh):
    return jax.shard_map(
        body_inner,
        mesh=mesh,
        in_specs=(
            P("pipe", "dp", "ctx", None),
            P("pipe", "dp", "ctx", None),
            P("pipe", "dp", "ctx", None),
            P("pipe", "dp", "ctx", None),
            P("dp", None),
        ),
        out_specs=(
            P("pipe", "dp", "ctx", None),
            P("pipe", "dp", "ctx", None),
            P("pipe", "dp", "ctx", None),
            P("pipe", None),
        ),
        check_vma=False,
    )
```

```python
import math

import jax
import jax.numpy as jnp
from jax import lax
from jax.sharding import PartitionSpec as P


ASKER_STREAMS = 32
SHARED_GROUPS = 4
FEATURE_SIZE = 128
QUERY_PER_KEY = 8
DOC_MOST = 512


def passed_along(value, axis, steps):
    count = lax.axis_size(axis)
    pairs = [(source, (source + steps) % count) for source in range(count)]
    return lax.ppermute(value, axis, pairs)


def shifted(value, axis, steps):
    count = lax.axis_size(axis)
    pairs = [(source, source + steps) for source in range(count) if 0 <= source + steps < count]
    return lax.ppermute(value, axis, pairs)


def radix_rounds(count):
    rounds, stride = [], 1
    while stride < count:
        radix = 4 if count % (stride * 4) == 0 else 2
        rounds.append((stride, radix))
        stride *= radix
    return rounds


def group_sum(value, axis):
    count = lax.axis_size(axis)
    if count & (count - 1):
        return lax.psum(value, axis)
    here = lax.axis_index(axis)
    for stride, radix in radix_rounds(count):
        got = [value] + [
            lax.ppermute(value, axis, [(i, i ^ (t * stride)) for i in range(count)])
            for t in range(1, radix)
        ]
        stack = jnp.stack(got)
        spot = (here // stride) % radix
        ordered = jnp.take(stack, spot ^ jnp.arange(radix), axis=0)
        while ordered.shape[0] > 1:
            ordered = ordered[0::2] + ordered[1::2]
        value = ordered[0]
    return value


def exchange_sum(value, axes):
    count = 1
    for axis in axes:
        count *= lax.axis_size(axis)
    if value.shape[0] % count:
        return group_sum(group_sum(value, axes[0]), axes[1])
    pieces = lax.all_to_all(value.reshape(count, -1), axes, 0, 0, tiled=True)
    ordered = pieces
    while ordered.shape[0] > 1:
        if ordered.shape[0] % 2:
            ordered = jnp.concatenate([ordered[:1] + ordered[1:2], ordered[2:]])
        else:
            ordered = ordered[0::2] + ordered[1::2]
    mine = jnp.broadcast_to(ordered, (count, ordered.shape[1]))
    return lax.all_to_all(mine, axes, 0, 0, tiled=True).reshape(-1)


def attend_group(query_g, key_g, value_g, cot_g, visible, scaling):
    scores = (
        jnp.einsum("qhd,kd->hqk", query_g, key_g, preferred_element_type=jnp.float32) * scaling
    )
    scores = jnp.where(visible[None], scores, -1e30)
    row_max = jnp.max(scores, axis=-1, keepdims=True)
    weights = jnp.where(visible[None], jnp.exp(scores - row_max), 0.0)
    probs = weights / jnp.sum(weights, axis=-1, keepdims=True)
    probs_b = probs.astype(jnp.bfloat16)
    attn_out = jnp.einsum("hqk,kd->qhd", probs_b, value_g, preferred_element_type=jnp.float32)
    dot_out = jnp.sum(cot_g.astype(jnp.float32) * attn_out, axis=-1).T[:, :, None]
    grad_prob = jnp.einsum("qhd,kd->hqk", cot_g, value_g, preferred_element_type=jnp.float32)
    grad_score = (probs * (grad_prob - dot_out) * scaling).astype(jnp.bfloat16)
    asker = jnp.einsum("hqk,kd->qhd", grad_score, key_g, preferred_element_type=jnp.float32)
    lookup = jnp.einsum("hqk,qhd->kd", grad_score, query_g, preferred_element_type=jnp.float32)
    content = jnp.einsum("hqk,qhd->kd", probs_b, cot_g, preferred_element_type=jnp.float32)
    return asker, lookup, content


def body_inner(queries, key_input, value_input, incoming, segments):
    shard_length = queries.shape[2]
    ctx_size = lax.axis_size("ctx")
    reach = min(-(-(DOC_MOST - 1) // shard_length), ctx_size - 1)
    window = (reach + 1) * shard_length
    width = SHARED_GROUPS * FEATURE_SIZE
    scaling = 1.0 / math.sqrt(FEATURE_SIZE)
    here = lax.axis_index("ctx")
    anchor = here * shard_length

    group_cols = QUERY_PER_KEY * FEATURE_SIZE
    per_chunk = SHARED_GROUPS
    chunk_cols = per_chunk * group_cols
    cot_chunks = [
        passed_along(incoming[0, 0, :, k * chunk_cols : (k + 1) * chunk_cols], "pipe", -1)
        for k in range(SHARED_GROUPS // per_chunk)
    ]
    cot_groups = [
        cot_chunks[g // per_chunk][:, (g % per_chunk) * group_cols : (g % per_chunk + 1) * group_cols]
        for g in range(SHARED_GROUPS)
    ]
    kv_own = jnp.concatenate([key_input[0, 0], value_input[0, 0]], axis=1)
    kv_window = jnp.concatenate(
        [shifted(kv_own, "ctx", steps) for steps in range(reach, 0, -1)] + [kv_own], axis=0
    )

    doc_ids = segments[0]
    doc_pad = jnp.concatenate([jnp.full((reach * shard_length,), -1, jnp.int32), doc_ids])
    key_doc = lax.dynamic_slice_in_dim(doc_pad, anchor, window, 0)
    query_doc = lax.dynamic_slice_in_dim(doc_ids, anchor, shard_length, 0)
    query_pos = jnp.arange(shard_length, dtype=jnp.int32) + reach * shard_length
    key_pos = jnp.arange(window, dtype=jnp.int32)
    visible = (query_doc[:, None] == key_doc[None, :]) & (key_pos[None, :] <= query_pos[:, None])

    query_tok = queries[0, 0].reshape(shard_length, ASKER_STREAMS, FEATURE_SIZE)
    askers, lookups, contents = [], [], []
    for group in range(SHARED_GROUPS):
        heads = slice(group * QUERY_PER_KEY, (group + 1) * QUERY_PER_KEY)
        cols = slice(group * FEATURE_SIZE, (group + 1) * FEATURE_SIZE)
        vcols = slice(width + group * FEATURE_SIZE, width + (group + 1) * FEATURE_SIZE)
        asker, lookup, content = attend_group(
            query_tok[:, heads],
            kv_window[:, cols],
            kv_window[:, vcols],
            cot_groups[group].reshape(shard_length, QUERY_PER_KEY, FEATURE_SIZE),
            visible,
            scaling,
        )
        askers.append(asker)
        lookups.append(lookup)
        contents.append(content)
    query_flat = jnp.concatenate(askers, axis=1).reshape(shard_length, ASKER_STREAMS * FEATURE_SIZE)
    grad_window = jnp.concatenate(lookups + contents, axis=1)

    offset_parts = jnp.concatenate([jnp.sum(query_flat, axis=0), jnp.sum(grad_window, axis=0)])

    grad_own = grad_window[reach * shard_length :]
    for block in range(reach):
        steps = reach - block
        part = grad_window[block * shard_length : (block + 1) * shard_length]
        grad_own = grad_own + shifted(part.astype(jnp.bfloat16), "ctx", -steps).astype(jnp.float32)

    offset_overall = exchange_sum(offset_parts, ("ctx", "dp"))
    bias_scaled = offset_overall / math.sqrt(lax.axis_size("dp") * shard_length * ctx_size)

    query_grad = query_flat.astype(jnp.bfloat16)[None, None]
    key_grad = grad_own[:, :width].astype(jnp.bfloat16)[None, None]
    value_grad = grad_own[:, width:].astype(jnp.bfloat16)[None, None]
    return (query_grad, key_grad, value_grad, bias_scaled[None])


def solution(mesh):
    return jax.shard_map(
        body_inner,
        mesh=mesh,
        in_specs=(
            P("pipe", "dp", "ctx", None),
            P("pipe", "dp", "ctx", None),
            P("pipe", "dp", "ctx", None),
            P("pipe", "dp", "ctx", None),
            P("dp", None),
        ),
        out_specs=(
            P("pipe", "dp", "ctx", None),
            P("pipe", "dp", "ctx", None),
            P("pipe", "dp", "ctx", None),
            P("pipe", None),
        ),
        check_vma=False,
    )
```
